128 devices in a mesh: dp: 16 (over x, z_lo, core), ctx: 8 (over z_hi, y).
Axes of the slice: x: 4, y: 4, z: 4 (z_hi: 2, z_lo: 2; z = z_hi * 2 + z_lo), core: 2. Of those that a mesh axis runs over, the one named last changes fastest.
Arguments:
- query_rows: bfloat16 [16, 2048, 2048], P('dp', 'ctx'), may hold values from -6 to 6
- key_rows: bfloat16 [16, 2048, 2048], P('dp', 'ctx'), may hold values from -6 to 6
- value_rows: bfloat16 [16, 2048, 2048], P('dp', 'ctx'), may hold values from -6 to 6
- utt_lengths: int32 [16, 8], P('dp'), may hold values from 1 to 1024, 2048 in all within a row
- out_weight: bfloat16 [2048, 4096], P('dp'), may hold values from -0.5 to 0.5
Outputs:
- out_rows: bfloat16 [16, 2048, 4096], P('dp', 'ctx')
The draws below stay inside these ranges and needn't reach their ends.
Inputs may be any that keep to these rules, and one draw needn't show every extreme that they name: `utt_lengths`: the 8 lengths of each sequence sum to 2048, and in each sequence one utterance has exactly 1024 frames.
All inputs are finite; a program needn't handle non-finite values.
Results may differ from the reference program's by a relative error of at most 0.015.
Values may be sent and summed in bfloat16 or wider, within the bound.
No kernel may reach another device: no remote copies, remote signals or barrier semaphores. Data moves between devices by JAX's collectives and lax.ppermute only.
A program may use at most 192 MiB of HBM per device.

```python
import math
import jax
import jax.numpy as jnp
import numpy as np
from jax import lax

D = 4096
HQ = 16
HD = 128
SEQS = 16
L = 2048
UTTS = 8
W = 2048


def draw_query_rows(key, part):
    noise_draw = jnp.clip(jax.random.normal(jax.random.fold_in(key, 11), (SEQS, L, HQ * HD), jnp.float32), -6.0, 6.0)
    return noise_draw.astype(jnp.bfloat16)


def draw_key_rows(key, part):
    noise_draw = jnp.clip(jax.random.normal(jax.random.fold_in(key, 23), (SEQS, L, HQ * HD), jnp.float32), -6.0, 6.0)
    return noise_draw.astype(jnp.bfloat16)


def levels(stream_key, extent, cuts, least, largest):
    def one(dim, shards_of):
        heights = jax.random.uniform(jax.random.fold_in(jax.random.fold_in(stream_key, 6), dim), (shards_of,), jnp.float32, least / len(cuts), largest / len(cuts))
        return jnp.repeat(jnp.exp(heights), extent[dim] // shards_of).reshape((-1,) + (1,) * (len(extent) - dim - 1))

    gain = one(*cuts[0])
    for cut in cuts[1:]:
        gain = gain * one(*cut)
    return gain


def split_up(amount, total, reach, skew):
    weights = [(1 << 20) // math.isqrt(standing ** skew) + 1 for standing in range(2, amount + 1)]
    rest, holding = total - reach - (amount - 1), [1] * (amount - 1)
    while rest > 0:
        free = [i for i in range(amount - 1) if holding[i] < reach]
        pool, left = sum([weights[i] for i in free]), rest
        for i in free:
            more = min(reach - holding[i], max(1, left * weights[i] // pool), rest)
            holding[i] = holding[i] + more
            rest = rest - more
    return np.array([reach] + holding)


def uneven_parts(own_key, count, total, reach, lean):
    if count == 2:
        one = jax.random.randint(own_key, (), max(1, total - reach), min(reach, total - 1) + 1)
        return jnp.stack([one, total - one])
    tallies = jnp.asarray(split_up(count, total, reach, lean), jnp.int32)
    couples = (count - 1) // 2
    donor, taker = tallies[1:1 + 2 * couples:2], tallies[2:2 + 2 * couples:2]
    slack = jnp.minimum(donor - 1, reach - taker)
    moved = jax.random.randint(jax.random.fold_in(own_key, 1), (couples,), 0, 1 << 20) % (slack + 1)
    tallies = tallies.at[1:1 + 2 * couples:2].set(donor - moved).at[2:2 + 2 * couples:2].set(taker + moved)
    return tallies[jax.random.permutation(jax.random.fold_in(own_key, 2), count)]


def centred(key, dims, scale, limit, cuts=(), held_as=jnp.bfloat16):
    entries = jax.random.normal(key, dims, jnp.float32) * scale
    if len(cuts) > 0:
        entries = levels(key, dims, cuts, -0.22, 0.18) * entries
    return jnp.clip(entries, min=-limit, max=limit).astype(held_as)


def setup_inputs(seed: int = 0) -> dict:
    seeds = jax.random.split(jax.random.key(seed), 6)
    return {
        "query_rows": draw_query_rows(jax.random.fold_in(seeds[5], 71), 0),
        "key_rows": draw_key_rows(jax.random.fold_in(seeds[5], 71), 0),
        "value_rows": centred(seeds[2], (SEQS, L, W), 1.0, 6.0, ((0, 16), (1, 8))),
        "utt_lengths": jax.vmap(lambda own: uneven_parts(own, UTTS, L, L // 2, 2))(jax.random.split(seeds[3], SEQS)).reshape((SEQS, UTTS)).astype(jnp.int32),
        "out_weight": centred(seeds[4], (W, D), (W // 16) ** -0.5, 0.5, ((0, 16),)),
    }


def one_sequence(inputs_one):
    query_rows, key_rows, value_rows, utt_lengths = inputs_one
    utt_ends = jnp.cumsum(utt_lengths)
    positions = jnp.arange(L, dtype=jnp.int32)
    segment = jnp.sum((positions[:, None] >= utt_ends[None, :]).astype(jnp.int32), axis=1)
    allowed = (segment[:, None] == segment[None, :])[:, None, :]
    query_heads = query_rows.reshape(L, HQ, HD).astype(jnp.float32)
    key_heads = key_rows.reshape(L, HQ, HD).astype(jnp.float32)
    value_heads = value_rows.reshape(L, HQ, HD).astype(jnp.float32)
    scores = jnp.einsum("qhd,khd->qhk", query_heads, key_heads) * (HD ** -0.5)
    masked = jnp.where(allowed, scores, -1.0e30)
    row_max = jnp.max(masked, axis=2)
    weights = jnp.where(allowed, jnp.exp(masked - row_max[:, :, None]), 0.0)
    denom = jnp.sum(weights, axis=2)
    rounded = lax.optimization_barrier(weights.astype(jnp.bfloat16)).astype(jnp.float32)
    numerator = jnp.einsum("qhk,khd->qhd", rounded, value_heads)
    return (numerator / denom[:, :, None]).reshape(L, HQ * HD).astype(jnp.bfloat16)


def reference(query_rows, key_rows, value_rows, utt_lengths, out_weight):
    def project(inputs_one):
        attn_rows = one_sequence(inputs_one)
        return jnp.dot(attn_rows, out_weight, preferred_element_type=jnp.float32).astype(jnp.bfloat16)

    return lax.map(project, (query_rows, key_rows, value_rows, utt_lengths))
```

```python
import jax
import jax.numpy as jnp
from jax import lax
from jax.sharding import PartitionSpec as P

HQ = 16
HD = 128


big_negative = -1e30


def from_behind(block, axis, distance):
    devices = range(lax.axis_size(axis))
    route = [((i - distance) % len(devices), i) for i in devices]
    return lax.ppermute(block, axis, route)


def segment_ids(utt_ends, first_frame, frames):
    positions = first_frame + jnp.arange(frames, dtype=jnp.int32)
    return jnp.sum((positions[:, None] >= utt_ends[None, :]).astype(jnp.int32), axis=1)


def attend(carry_state, query_heads, query_seg, kv_block, key_seg):
    max_old, denom_old, numerator = carry_state
    frames = kv_block.shape[1]
    key_heads = kv_block[0].reshape(frames, HQ, HD)
    value_heads = kv_block[1].reshape(frames, HQ, HD)
    allowed = (query_seg[:, None] == key_seg[None, :])[:, None, :]
    scores = jnp.einsum(
        "qhd,khd->qhk", query_heads, key_heads, preferred_element_type=jnp.float32
    ) * HD ** (-0.5)
    masked = jnp.where(allowed, scores, big_negative)
    max_new = jnp.maximum(max_old, jnp.max(masked, axis=2))
    weights = jnp.where(allowed, jnp.exp(masked - max_new[:, :, None]), 0.0)
    rescale = jnp.exp(max_old - max_new)
    denom_new = denom_old * rescale + jnp.sum(weights, axis=2)
    numerator = numerator * rescale[:, :, None] + jnp.einsum(
        "qhk,khd->qhd",
        weights.astype(jnp.bfloat16),
        value_heads,
        preferred_element_type=jnp.float32,
    )
    return (max_new, denom_new, numerator)


def shards(query_rows, key_rows, value_rows, utt_lengths, out_weight):
    frames = query_rows.shape[1]
    cycle_size = lax.axis_size("ctx")
    cycle_place = lax.axis_index("ctx")
    utt_ends = jnp.cumsum(utt_lengths[0])
    query_heads = query_rows[0].reshape(frames, HQ, HD)
    query_seg = segment_ids(utt_ends, cycle_place * frames, frames)

    def absorb(carry_state, kv_block, source):
        key_seg = segment_ids(utt_ends, source * frames, frames)
        return attend(carry_state, query_heads, query_seg, kv_block, key_seg)

    initial = (
        jnp.full((frames, HQ), big_negative, jnp.float32),
        jnp.zeros((frames, HQ), jnp.float32),
        jnp.zeros((frames, HQ, HD), jnp.float32),
    )
    gathered_weight = lax.all_gather(out_weight, "dp", axis=0, tiled=True)
    kv_block = jnp.concatenate([key_rows, value_rows], axis=0)
    carry_state = absorb(initial, kv_block, cycle_place)
    ahead = kv_block
    behind = kv_block
    for hop_index in range(1, cycle_size // 2 + 1):
        ahead = from_behind(ahead, "ctx", 1)
        if hop_index < cycle_size - cycle_size // 2:
            behind = from_behind(behind, "ctx", -1)
        carry_state = absorb(carry_state, ahead, (cycle_place - hop_index) % cycle_size)
        if hop_index < cycle_size - cycle_size // 2:
            carry_state = absorb(carry_state, behind, (cycle_place + hop_index) % cycle_size)
    max_final, denom_final, numerator = carry_state
    attn_rows = (numerator / denom_final[:, :, None]).reshape(frames, HQ * HD).astype(jnp.bfloat16)
    summed = jnp.dot(
        attn_rows,
        gathered_weight,
        preferred_element_type=jnp.float32,
    )
    return summed.astype(jnp.bfloat16)[None]


def solution(mesh):
    return jax.shard_map(
        shards,
        mesh=mesh,
        in_specs=(
            P("dp", "ctx", None),
            P("dp", "ctx", None),
            P("dp", "ctx", None),
            P("dp", None),
            P("dp", None),
        ),
        out_specs=P("dp", "ctx", None),
        check_vma=False,
    )
```

```python
import jax
import jax.numpy as jnp
from jax import lax
from jax.sharding import PartitionSpec as P

HQ = 16
HD = 128


big_negative = -1e30


def segment_ids(utt_ends, first_frame, frames):
    positions = first_frame + jnp.arange(frames, dtype=jnp.int32)
    return jnp.sum((positions[:, None] >= utt_ends[None, :]).astype(jnp.int32), axis=1)


def attend(carry_state, query_heads, query_seg, kv_block, key_seg):
    max_old, denom_old, numerator = carry_state
    frames = kv_block.shape[1]
    key_heads = kv_block[0].reshape(frames, HQ, HD)
    value_heads = kv_block[1].reshape(frames, HQ, HD)
    allowed = (query_seg[:, None] == key_seg[None, :])[:, None, :]
    scores = jnp.einsum(
        "qhd,khd->qhk", query_heads, key_heads, preferred_element_type=jnp.float32
    ) * HD ** (-0.5)
    masked = jnp.where(allowed, scores, big_negative)
    max_new = jnp.maximum(max_old, jnp.max(masked, axis=2))
    weights = jnp.where(allowed, jnp.exp(masked - max_new[:, :, None]), 0.0)
    rescale = jnp.exp(max_old - max_new)
    denom_new = denom_old * rescale + jnp.sum(weights, axis=2)
    numerator = numerator * rescale[:, :, None] + jnp.einsum(
        "qhk,khd->qhd",
        weights.astype(jnp.bfloat16),
        value_heads,
        preferred_element_type=jnp.float32,
    )
    return (max_new, denom_new, numerator)


def shards(query_rows, key_rows, value_rows, utt_lengths, out_weight):
    frames = query_rows.shape[1]
    cycle_size = lax.axis_size("ctx")
    cycle_place = lax.axis_index("ctx")
    utt_ends = jnp.cumsum(utt_lengths[0])
    query_heads = query_rows[0].reshape(frames, HQ, HD)
    query_seg = segment_ids(utt_ends, cycle_place * frames, frames)

    def absorb(carry_state, kv_block, source):
        key_seg = segment_ids(utt_ends, source * frames, frames)
        return attend(carry_state, query_heads, query_seg, kv_block, key_seg)

    initial = (
        jnp.full((frames, HQ), big_negative, jnp.float32),
        jnp.zeros((frames, HQ), jnp.float32),
        jnp.zeros((frames, HQ, HD), jnp.float32),
    )
    gathered_weight = lax.all_gather(out_weight, "dp", axis=0, tiled=True)
    kv_block = jnp.concatenate([key_rows, value_rows], axis=0)
    plane_size = cycle_size // 2
    plane = cycle_place // plane_size
    spot = cycle_place % plane_size
    half = frames // 2

    def in_plane(block, step):
        route = [
            (i, (i // plane_size) * plane_size + (i % plane_size + step) % plane_size)
            for i in range(cycle_size)
        ]
        return lax.ppermute(block, "ctx", route)

    def around(block, source_plane):
        ahead = in_plane(block, 1)
        behind = in_plane(block, -1)
        ahead_two = in_plane(ahead[:, :half], 1)
        behind_two = in_plane(behind[:, half:], -1)
        far = jnp.concatenate([ahead_two, behind_two], axis=1)
        base = source_plane * plane_size
        return [
            (ahead, base + (spot - 1) % plane_size),
            (behind, base + (spot + 1) % plane_size),
            (far, base + (spot + 2) % plane_size),
        ]

    partner = lax.ppermute(
        kv_block, "ctx", [(i, (i + plane_size) % cycle_size) for i in range(cycle_size)]
    )
    arrivals = [(kv_block, cycle_place)] + around(kv_block, plane)
    arrivals += [(partner, (cycle_place + plane_size) % cycle_size)]
    arrivals += around(partner, 1 - plane)
    carry_state = initial
    for block, source in arrivals:
        carry_state = absorb(carry_state, block, source)
    max_final, denom_final, numerator = carry_state
    attn_rows = (numerator / denom_final[:, :, None]).reshape(frames, HQ * HD).astype(jnp.bfloat16)
    summed = jnp.dot(
        attn_rows,
        gathered_weight,
        preferred_element_type=jnp.float32,
    )
    return summed.astype(jnp.bfloat16)[None]


def solution(mesh):
    return jax.shard_map(
        shards,
        mesh=mesh,
        in_specs=(
            P("dp", "ctx", None),
            P("dp", "ctx", None),
            P("dp", "ctx", None),
            P("dp", None),
            P("dp", None),
        ),
        out_specs=P("dp", "ctx", None),
        check_vma=False,
    )
```

```python
import jax
import jax.numpy as jnp
from jax import lax
from jax.sharding import PartitionSpec as P

HQ = 16
HD = 128


big_negative = -1e30


def segment_ids(utt_ends, first_frame, frames):
    positions = first_frame + jnp.arange(frames, dtype=jnp.int32)
    return jnp.sum((positions[:, None] >= utt_ends[None, :]).astype(jnp.int32), axis=1)


def attend(carry_state, query_heads, query_seg, kv_block, key_seg):
    max_old, denom_old, numerator = carry_state
    frames = kv_block.shape[1]
    key_heads = kv_block[0].reshape(frames, HQ, HD)
    value_heads = kv_block[1].reshape(frames, HQ, HD)
    allowed = (query_seg[:, None] == key_seg[None, :])[:, None, :]
    scores = jnp.einsum(
        "qhd,khd->qhk", query_heads, key_heads, preferred_element_type=jnp.float32
    ) * HD ** (-0.5)
    masked = jnp.where(allowed, scores, big_negative)
    max_new = jnp.maximum(max_old, jnp.max(masked, axis=2))
    weights = jnp.where(allowed, jnp.exp(masked - max_new[:, :, None]), 0.0)
    rescale = jnp.exp(max_old - max_new)
    denom_new = denom_old * rescale + jnp.sum(weights, axis=2)
    numerator = numerator * rescale[:, :, None] + jnp.einsum(
        "qhk,khd->qhd",
        weights.astype(jnp.bfloat16),
        value_heads,
        preferred_element_type=jnp.float32,
    )
    return (max_new, denom_new, numerator)


def shards(query_rows, key_rows, value_rows, utt_lengths, out_weight):
    frames = query_rows.shape[1]
    cycle_size = lax.axis_size("ctx")
    cycle_place = lax.axis_index("ctx")
    utt_ends = jnp.cumsum(utt_lengths[0])
    query_heads = query_rows[0].reshape(frames, HQ, HD)
    query_seg = segment_ids(utt_ends, cycle_place * frames, frames)

    def absorb(carry_state, kv_block, source):
        key_seg = segment_ids(utt_ends, source * frames, frames)
        return attend(carry_state, query_heads, query_seg, kv_block, key_seg)

    initial = (
        jnp.full((frames, HQ), big_negative, jnp.float32),
        jnp.zeros((frames, HQ), jnp.float32),
        jnp.zeros((frames, HQ, HD), jnp.float32),
    )
    gathered_weight = lax.all_gather(out_weight, "dp", axis=0, tiled=True)
    kv_block = jnp.concatenate([key_rows, value_rows], axis=0)
    plane_size = cycle_size // 2
    plane = cycle_place // plane_size
    spot = cycle_place % plane_size
    half = frames // 2

    def in_plane(block, step):
        route = [
            (i, (i // plane_size) * plane_size + (i % plane_size + step) % plane_size)
            for i in range(cycle_size)
        ]
        return lax.ppermute(block, "ctx", route)

    def around(block, source_plane):
        ahead = in_plane(block, 1)
        behind = in_plane(block, -1)
        ahead_two = in_plane(ahead[:, :half], 1)
        behind_two = in_plane(behind[:, half:], -1)
        far = jnp.concatenate([ahead_two, behind_two], axis=1)
        base = source_plane * plane_size
        return [
            (ahead, base + (spot - 1) % plane_size),
            (behind, base + (spot + 1) % plane_size),
            (far, base + (spot + 2) % plane_size),
        ]

    partner = lax.ppermute(
        kv_block, "ctx", [(i, (i + plane_size) % cycle_size) for i in range(cycle_size)]
    )
    arrivals = [(kv_block, cycle_place)] + around(kv_block, plane)
    arrivals += [(partner, (cycle_place + plane_size) % cycle_size)]
    arrivals += around(partner, 1 - plane)
    carry_state = initial
    for block, source in arrivals:
        carry_state = lax.optimization_barrier(absorb(carry_state, block, source))
    max_final, denom_final, numerator = carry_state
    attn_rows = (numerator / denom_final[:, :, None]).reshape(frames, HQ * HD).astype(jnp.bfloat16)
    summed = jnp.dot(
        attn_rows,
        gathered_weight,
        preferred_element_type=jnp.float32,
    )
    return summed.astype(jnp.bfloat16)[None]


def solution(mesh):
    return jax.shard_map(
        shards,
        mesh=mesh,
        in_specs=(
            P("dp", "ctx", None),
            P("dp", "ctx", None),
            P("dp", "ctx", None),
            P("dp", None),
            P("dp", None),
        ),
        out_specs=P("dp", "ctx", None),
        check_vma=False,
    )
```

```python
import jax
import jax.numpy as jnp
from jax import lax
from jax.sharding import PartitionSpec as P

HQ = 16
HD = 128


big_negative = -1e30


def z_hop(block, step):
    dp_size = lax.axis_size("dp")
    ctx_size = lax.axis_size("ctx")
    route = []
    for d in range(dp_size):
        for c in range(ctx_size):
            z = 2 * (c // (ctx_size // 2)) + (d // 2) % 2
            nz = (z + step) % 4
            nd = d - 2 * ((d // 2) % 2) + 2 * (nz % 2)
            nc = (nz // 2) * (ctx_size // 2) + c % (ctx_size // 2)
            route.append((d * ctx_size + c, nd * ctx_size + nc))
    return lax.ppermute(block, ("dp", "ctx"), route)


def segment_ids(utt_ends, first_frame, frames):
    positions = first_frame + jnp.arange(frames, dtype=jnp.int32)
    return jnp.sum((positions[:, None] >= utt_ends[None, :]).astype(jnp.int32), axis=1)


def attend(carry_state, query_heads, query_seg, kv_block, key_seg):
    max_old, denom_old, numerator = carry_state
    frames = kv_block.shape[1]
    key_heads = kv_block[0].reshape(frames, HQ, HD)
    value_heads = kv_block[1].reshape(frames, HQ, HD)
    allowed = (query_seg[:, None] == key_seg[None, :])[:, None, :]
    scores = jnp.einsum(
        "qhd,khd->qhk", query_heads, key_heads, preferred_element_type=jnp.float32
    ) * HD ** (-0.5)
    masked = jnp.where(allowed, scores, big_negative)
    max_new = jnp.maximum(max_old, jnp.max(masked, axis=2))
    weights = jnp.where(allowed, jnp.exp(masked - max_new[:, :, None]), 0.0)
    rescale = jnp.exp(max_old - max_new)
    denom_new = denom_old * rescale + jnp.sum(weights, axis=2)
    numerator = numerator * rescale[:, :, None] + jnp.einsum(
        "qhk,khd->qhd",
        weights.astype(jnp.bfloat16),
        value_heads,
        preferred_element_type=jnp.float32,
    )
    return (max_new, denom_new, numerator)


def shards(query_rows, key_rows, value_rows, utt_lengths, out_weight):
    frames = query_rows.shape[1]
    cycle_size = lax.axis_size("ctx")
    cycle_place = lax.axis_index("ctx")
    utt_ends = jnp.cumsum(utt_lengths[0])
    query_heads = query_rows[0].reshape(frames, HQ, HD)
    query_seg = segment_ids(utt_ends, cycle_place * frames, frames)

    def absorb(carry_state, kv_block, source):
        key_seg = segment_ids(utt_ends, source * frames, frames)
        return attend(carry_state, query_heads, query_seg, kv_block, key_seg)

    initial = (
        jnp.full((frames, HQ), big_negative, jnp.float32),
        jnp.zeros((frames, HQ), jnp.float32),
        jnp.zeros((frames, HQ, HD), jnp.float32),
    )
    gathered_weight = lax.all_gather(out_weight, "dp", axis=0, tiled=True)
    kv_block = jnp.concatenate([key_rows, value_rows], axis=0)
    plane_size = cycle_size // 2
    plane = cycle_place // plane_size
    spot = cycle_place % plane_size
    half = frames // 2

    def in_plane(block, step):
        route = [
            (i, (i // plane_size) * plane_size + (i % plane_size + step) % plane_size)
            for i in range(cycle_size)
        ]
        return lax.ppermute(block, "ctx", route)

    def around(block, source_plane):
        ahead = in_plane(block, 1)
        behind = in_plane(block, -1)
        ahead_two = in_plane(ahead[:, :half], 1)
        behind_two = in_plane(behind[:, half:], -1)
        far = jnp.concatenate([ahead_two, behind_two], axis=1)
        base = source_plane * plane_size
        return [
            (ahead, base + (spot - 1) % plane_size),
            (behind, base + (spot + 1) % plane_size),
            (far, base + (spot + 2) % plane_size),
        ]

    lower_half = kv_block[:, :half]
    upper_half = kv_block[:, half:]
    for hop in range(2):
        lower_half = z_hop(lower_half, 1)
        upper_half = z_hop(upper_half, -1)
    partner = jnp.concatenate([lower_half, upper_half], axis=1)
    arrivals = [(kv_block, cycle_place)] + around(kv_block, plane)
    arrivals += [(partner, (cycle_place + plane_size) % cycle_size)]
    arrivals += around(partner, 1 - plane)
    carry_state = initial
    for block, source in arrivals:
        carry_state = lax.optimization_barrier(absorb(carry_state, block, source))
    max_final, denom_final, numerator = carry_state
    attn_rows = (numerator / denom_final[:, :, None]).reshape(frames, HQ * HD).astype(jnp.bfloat16)
    summed = jnp.dot(
        attn_rows,
        gathered_weight,
        preferred_element_type=jnp.float32,
    )
    return summed.astype(jnp.bfloat16)[None]


def solution(mesh):
    return jax.shard_map(
        shards,
        mesh=mesh,
        in_specs=(
            P("dp", "ctx", None),
            P("dp", "ctx", None),
            P("dp", "ctx", None),
            P("dp", None),
            P("dp", None),
        ),
        out_specs=P("dp", "ctx", None),
        check_vma=False,
    )
```

```python
import jax
import jax.numpy as jnp
from jax import lax
from jax.sharding import PartitionSpec as P

HQ = 16
HD = 128


big_negative = -1e30


def segment_ids(utt_ends, first_frame, frames):
    positions = first_frame + jnp.arange(frames, dtype=jnp.int32)
    return jnp.sum((positions[:, None] >= utt_ends[None, :]).astype(jnp.int32), axis=1)


def attend(carry_state, query_heads, query_seg, kv_block, key_seg):
    max_old, denom_old, numerator = carry_state
    frames = kv_block.shape[1]
    key_heads = kv_block[0].reshape(frames, -1, HD)
    value_heads = kv_block[1].reshape(frames, -1, HD)
    allowed = (query_seg[:, None] == key_seg[None, :])[:, None, :]
    scores = jnp.einsum(
        "qhd,khd->qhk", query_heads, key_heads, preferred_element_type=jnp.float32
    ) * HD ** (-0.5)
    masked = jnp.where(allowed, scores, big_negative)
    max_new = jnp.maximum(max_old, jnp.max(masked, axis=2))
    weights = jnp.where(allowed, jnp.exp(masked - max_new[:, :, None]), 0.0)
    rescale = jnp.exp(max_old - max_new)
    denom_new = denom_old * rescale + jnp.sum(weights, axis=2)
    numerator = numerator * rescale[:, :, None] + jnp.einsum(
        "qhk,khd->qhd",
        weights.astype(jnp.bfloat16),
        value_heads,
        preferred_element_type=jnp.float32,
    )
    return (max_new, denom_new, numerator)


def shards(query_rows, key_rows, value_rows, utt_lengths, out_weight):
    frames = query_rows.shape[1]
    cycle_size = lax.axis_size("ctx")
    cycle_place = lax.axis_index("ctx")
    utt_ends = jnp.cumsum(utt_lengths[0])
    query_heads = query_rows[0].reshape(frames, HQ, HD)
    query_seg = segment_ids(utt_ends, cycle_place * frames, frames)

    def absorb(carry_state, kv_block, source, heads=slice(None)):
        key_seg = segment_ids(utt_ends, source * frames, frames)
        return attend(carry_state, query_heads[:, heads], query_seg, kv_block, key_seg)

    initial = (
        jnp.full((frames, HQ), big_negative, jnp.float32),
        jnp.zeros((frames, HQ), jnp.float32),
        jnp.zeros((frames, HQ, HD), jnp.float32),
    )
    gathered_weight = lax.all_gather(out_weight, "dp", axis=0, tiled=True)
    kv_block = jnp.concatenate([key_rows, value_rows], axis=0)
    plane_size = cycle_size // 2
    plane = cycle_place // plane_size
    spot = cycle_place % plane_size
    half = frames // 2

    def in_plane(block, step):
        route = [
            (i, (i // plane_size) * plane_size + (i % plane_size + step) % plane_size)
            for i in range(cycle_size)
        ]
        return lax.ppermute(block, "ctx", route)

    def around(block, source_plane):
        ahead = in_plane(block, 1)
        behind = in_plane(block, -1)
        ahead_two = in_plane(ahead[:, :half], 1)
        behind_two = in_plane(behind[:, half:], -1)
        far = jnp.concatenate([ahead_two, behind_two], axis=1)
        base = source_plane * plane_size
        return [
            (ahead, base + (spot - 1) % plane_size),
            (behind, base + (spot + 1) % plane_size),
            (far, base + (spot + 2) % plane_size),
        ]

    partner = lax.ppermute(
        kv_block, "ctx", [(i, (i + plane_size) % cycle_size) for i in range(cycle_size)]
    )
    arrivals = [(kv_block, cycle_place)] + around(kv_block, plane)
    arrivals += [(partner, (cycle_place + plane_size) % cycle_size)]
    partner_ahead = in_plane(partner, 1)
    partner_behind = in_plane(partner, -1)
    arrivals += [
        (partner_ahead, (1 - plane) * plane_size + (spot - 1) % plane_size),
        (partner_behind, (1 - plane) * plane_size + (spot + 1) % plane_size),
    ]
    carry_state = initial
    for block, source in arrivals:
        carry_state = lax.optimization_barrier(absorb(carry_state, block, source))
    far_source = (1 - plane) * plane_size + (spot + 2) % plane_size
    groups = 2
    width = HQ // groups
    pieces = []
    for group in range(groups):
        cols = slice(group * width * HD, (group + 1) * width * HD)
        pieces.append(
            (
                in_plane(partner_ahead[:, :half, cols], 1),
                in_plane(partner_behind[:, half:, cols], -1),
            )
        )
    summed = None
    for group in range(groups):
        heads = slice(group * width, (group + 1) * width)
        cols = slice(group * width * HD, (group + 1) * width * HD)
        if summed is not None:
            summed, pieces[group] = lax.optimization_barrier((summed, pieces[group]))
        far = jnp.concatenate(pieces[group], axis=1)
        group_state = tuple(part[:, heads] for part in carry_state)
        max_final, denom_final, numerator = absorb(group_state, far, far_source, heads)
        attn_rows = (numerator / denom_final[:, :, None]).reshape(frames, width * HD)
        partial = jnp.dot(
            attn_rows.astype(jnp.bfloat16),
            gathered_weight[cols],
            preferred_element_type=jnp.float32,
        )
        summed = partial if summed is None else summed + partial
    return summed.astype(jnp.bfloat16)[None]


def solution(mesh):
    return jax.shard_map(
        shards,
        mesh=mesh,
        in_specs=(
            P("dp", "ctx", None),
            P("dp", "ctx", None),
            P("dp", "ctx", None),
            P("dp", None),
            P("dp", None),
        ),
        out_specs=P("dp", "ctx", None),
        check_vma=False,
    )
```

```python
import jax
import jax.numpy as jnp
from jax import lax
from jax.sharding import PartitionSpec as P

HQ = 16
HD = 128


big_negative = -1e30


def segment_ids(utt_ends, first_frame, frames):
    positions = first_frame + jnp.arange(frames, dtype=jnp.int32)
    return jnp.sum((positions[:, None] >= utt_ends[None, :]).astype(jnp.int32), axis=1)


def attend(carry_state, query_heads, query_seg, kv_block, key_seg, first=False):
    max_old, denom_old, numerator = carry_state
    frames = kv_block.shape[1]
    key_heads = kv_block[0].reshape(frames, -1, HD)
    value_heads = kv_block[1].reshape(frames, -1, HD)
    allowed = (query_seg[:, None] == key_seg[None, :])[:, None, :]
    scores = jnp.einsum(
        "qhd,khd->qhk", query_heads, key_heads, preferred_element_type=jnp.float32
    ) * HD ** (-0.5)
    masked = jnp.where(allowed, scores, big_negative)
    max_new = jnp.maximum(max_old, jnp.max(masked, axis=2))
    weights = jnp.exp(masked - max_new[:, :, None])
    if first:
        weights = jnp.where(allowed, weights, 0.0)
    rescale = jnp.exp(max_old - max_new)
    denom_new = denom_old * rescale + jnp.sum(weights, axis=2)
    numerator = numerator * rescale[:, :, None] + jnp.einsum(
        "qhk,khd->qhd",
        weights.astype(jnp.bfloat16),
        value_heads,
        preferred_element_type=jnp.float32,
    )
    return (max_new, denom_new, numerator)


def shards(query_rows, key_rows, value_rows, utt_lengths, out_weight):
    frames = query_rows.shape[1]
    cycle_size = lax.axis_size("ctx")
    cycle_place = lax.axis_index("ctx")
    utt_ends = jnp.cumsum(utt_lengths[0])
    query_heads = query_rows[0].reshape(frames, HQ, HD)
    query_seg = segment_ids(utt_ends, cycle_place * frames, frames)

    def absorb(carry_state, kv_block, source, heads=slice(None)):
        key_seg = segment_ids(utt_ends, source * frames, frames)
        return attend(carry_state, query_heads[:, heads], query_seg, kv_block, key_seg)

    initial = (
        jnp.full((frames, HQ), big_negative, jnp.float32),
        jnp.zeros((frames, HQ), jnp.float32),
        jnp.zeros((frames, HQ, HD), jnp.float32),
    )
    gathered_weight = lax.all_gather(out_weight, "dp", axis=0, tiled=True)
    kv_block = jnp.concatenate([key_rows, value_rows], axis=0)
    plane_size = cycle_size // 2
    plane = cycle_place // plane_size
    spot = cycle_place % plane_size
    half = frames // 2

    def in_plane(block, step):
        route = [
            (i, (i // plane_size) * plane_size + (i % plane_size + step) % plane_size)
            for i in range(cycle_size)
        ]
        return lax.ppermute(block, "ctx", route)

    def around(block, source_plane):
        ahead = in_plane(block, 1)
        behind = in_plane(block, -1)
        ahead_two = in_plane(ahead[:, :half], 1)
        behind_two = in_plane(behind[:, half:], -1)
        far = jnp.concatenate([ahead_two, behind_two], axis=1)
        base = source_plane * plane_size
        return [
            (ahead, base + (spot - 1) % plane_size),
            (behind, base + (spot + 1) % plane_size),
            (far, base + (spot + 2) % plane_size),
        ]

    partner = lax.ppermute(
        kv_block, "ctx", [(i, (i + plane_size) % cycle_size) for i in range(cycle_size)]
    )
    arrivals = [(kv_block, cycle_place)] + around(kv_block, plane)
    arrivals += [(partner, (cycle_place + plane_size) % cycle_size)]
    partner_ahead = in_plane(partner, 1)
    partner_behind = in_plane(partner, -1)
    arrivals += [
        (partner_ahead, (1 - plane) * plane_size + (spot - 1) % plane_size),
        (partner_behind, (1 - plane) * plane_size + (spot + 1) % plane_size),
    ]
    carry_state = initial
    for block, source in arrivals:
        carry_state = lax.optimization_barrier(absorb(carry_state, block, source))
    far_source = (1 - plane) * plane_size + (spot + 2) % plane_size
    groups = 2
    width = HQ // groups
    pieces = []
    for group in range(groups):
        cols = slice(group * width * HD, (group + 1) * width * HD)
        pieces.append(
            (
                in_plane(partner_ahead[:, :half, cols], 1),
                in_plane(partner_behind[:, half:, cols], -1),
            )
        )
    summed = None
    for group in range(groups):
        heads = slice(group * width, (group + 1) * width)
        cols = slice(group * width * HD, (group + 1) * width * HD)
        if summed is not None:
            summed, pieces[group] = lax.optimization_barrier((summed, pieces[group]))
        far = jnp.concatenate(pieces[group], axis=1)
        group_state = tuple(part[:, heads] for part in carry_state)
        max_final, denom_final, numerator = absorb(group_state, far, far_source, heads)
        attn_rows = (numerator / denom_final[:, :, None]).reshape(frames, width * HD)
        partial = jnp.dot(
            attn_rows.astype(jnp.bfloat16),
            gathered_weight[cols],
            preferred_element_type=jnp.float32,
        )
        summed = partial if summed is None else summed + partial
    return summed.astype(jnp.bfloat16)[None]


def solution(mesh):
    return jax.shard_map(
        shards,
        mesh=mesh,
        in_specs=(
            P("dp", "ctx", None),
            P("dp", "ctx", None),
            P("dp", "ctx", None),
            P("dp", None),
            P("dp", None),
        ),
        out_specs=P("dp", "ctx", None),
        check_vma=False,
    )
```

```python
import jax
import jax.numpy as jnp
from jax import lax
from jax.sharding import PartitionSpec as P

HQ = 16
HD = 128


big_negative = -1e30


def segment_ids(utt_ends, first_frame, frames):
    positions = first_frame + jnp.arange(frames, dtype=jnp.int32)
    return jnp.sum((positions[:, None] >= utt_ends[None, :]).astype(jnp.int32), axis=1)


def attend(carry_state, query_heads, query_seg, kv_block, key_seg):
    frames = kv_block.shape[1]
    key_heads = kv_block[0].reshape(frames, -1, HD)
    value_heads = kv_block[1].reshape(frames, -1, HD)
    allowed = (query_seg[:, None] == key_seg[None, :])[:, None, :]
    scores = jnp.einsum(
        "qhd,khd->qhk", query_heads, key_heads, preferred_element_type=jnp.float32
    ) * HD ** (-0.5)
    masked = jnp.where(allowed, scores, big_negative)
    block_max = jnp.max(masked, axis=2)
    max_new = block_max if carry_state is None else jnp.maximum(carry_state[0], block_max)
    weights = jnp.exp(masked - max_new[:, :, None])
    denom_new = jnp.sum(weights, axis=2)
    numerator = jnp.einsum(
        "qhk,khd->qhd",
        weights.astype(jnp.bfloat16),
        value_heads,
        preferred_element_type=jnp.float32,
    )
    if carry_state is not None:
        max_old, denom_old, numerator_old = carry_state
        rescale = jnp.exp(max_old - max_new)
        denom_new = denom_old * rescale + denom_new
        numerator = numerator_old * rescale[:, :, None] + numerator
    return (max_new, denom_new, numerator)


def shards(query_rows, key_rows, value_rows, utt_lengths, out_weight):
    frames = query_rows.shape[1]
    cycle_size = lax.axis_size("ctx")
    cycle_place = lax.axis_index("ctx")
    utt_ends = jnp.cumsum(utt_lengths[0])
    query_heads = query_rows[0].reshape(frames, HQ, HD)
    query_seg = segment_ids(utt_ends, cycle_place * frames, frames)

    def absorb(carry_state, kv_block, source, heads=slice(None)):
        key_seg = segment_ids(utt_ends, source * frames, frames)
        return attend(carry_state, query_heads[:, heads], query_seg, kv_block, key_seg)

    gathered_weight = lax.all_gather(out_weight, "dp", axis=0, tiled=True)
    kv_block = jnp.concatenate([key_rows, value_rows], axis=0)
    plane_size = cycle_size // 2
    plane = cycle_place // plane_size
    spot = cycle_place % plane_size
    half = frames // 2

    def in_plane(block, step):
        route = [
            (i, (i // plane_size) * plane_size + (i % plane_size + step) % plane_size)
            for i in range(cycle_size)
        ]
        return lax.ppermute(block, "ctx", route)

    def around(block, source_plane):
        ahead = in_plane(block, 1)
        behind = in_plane(block, -1)
        ahead_two = in_plane(ahead[:, :half], 1)
        behind_two = in_plane(behind[:, half:], -1)
        far = jnp.concatenate([ahead_two, behind_two], axis=1)
        base = source_plane * plane_size
        return [
            (ahead, base + (spot - 1) % plane_size),
            (behind, base + (spot + 1) % plane_size),
            (far, base + (spot + 2) % plane_size),
        ]

    partner = lax.ppermute(
        kv_block, "ctx", [(i, (i + plane_size) % cycle_size) for i in range(cycle_size)]
    )
    arrivals = [(kv_block, cycle_place)] + around(kv_block, plane)
    arrivals += [(partner, (cycle_place + plane_size) % cycle_size)]
    partner_ahead = in_plane(partner, 1)
    partner_behind = in_plane(partner, -1)
    arrivals += [
        (partner_ahead, (1 - plane) * plane_size + (spot - 1) % plane_size),
        (partner_behind, (1 - plane) * plane_size + (spot + 1) % plane_size),
    ]
    carry_state = None
    for block, source in arrivals:
        carry_state = lax.optimization_barrier(absorb(carry_state, block, source))
    far_source = (1 - plane) * plane_size + (spot + 2) % plane_size
    groups = 2
    width = HQ // groups
    pieces = []
    for group in range(groups):
        cols = slice(group * width * HD, (group + 1) * width * HD)
        pieces.append(
            (
                in_plane(partner_ahead[:, :half, cols], 1),
                in_plane(partner_behind[:, half:, cols], -1),
            )
        )
    summed = None
    for group in range(groups):
        heads = slice(group * width, (group + 1) * width)
        cols = slice(group * width * HD, (group + 1) * width * HD)
        if summed is not None:
            summed, pieces[group] = lax.optimization_barrier((summed, pieces[group]))
        far = jnp.concatenate(pieces[group], axis=1)
        group_state = tuple(part[:, heads] for part in carry_state)
        max_final, denom_final, numerator = absorb(group_state, far, far_source, heads)
        attn_rows = (numerator / denom_final[:, :, None]).reshape(frames, width * HD)
        partial = jnp.dot(
            attn_rows.astype(jnp.bfloat16),
            gathered_weight[cols],
            preferred_element_type=jnp.float32,
        )
        summed = partial if summed is None else summed + partial
    return summed.astype(jnp.bfloat16)[None]


def solution(mesh):
    return jax.shard_map(
        shards,
        mesh=mesh,
        in_specs=(
            P("dp", "ctx", None),
            P("dp", "ctx", None),
            P("dp", "ctx", None),
            P("dp", None),
            P("dp", None),
        ),
        out_specs=P("dp", "ctx", None),
        check_vma=False,
    )
```

```python
import jax
import jax.numpy as jnp
from jax import lax
from jax.sharding import PartitionSpec as P

HQ = 16
HD = 128


big_negative = -1e30


def segment_ids(utt_ends, first_frame, frames):
    positions = first_frame + jnp.arange(frames, dtype=jnp.int32)
    return jnp.sum((positions[:, None] >= utt_ends[None, :]).astype(jnp.int32), axis=1)


def attend(carry_state, query_heads, query_seg, kv_pair, key_seg):
    keys, values = kv_pair
    frames = keys.shape[0]
    key_heads = keys.reshape(frames, -1, HD)
    value_heads = values.reshape(frames, -1, HD)
    allowed = (query_seg[:, None] == key_seg[None, :])[:, None, :]
    scores = jnp.einsum(
        "qhd,khd->qhk", query_heads, key_heads, preferred_element_type=jnp.float32
    ) * HD ** (-0.5)
    masked = jnp.where(allowed, scores, big_negative)
    block_max = jnp.max(masked, axis=2)
    max_new = block_max if carry_state is None else jnp.maximum(carry_state[0], block_max)
    weights = jnp.exp(masked - max_new[:, :, None])
    denom_new = jnp.sum(weights, axis=2)
    numerator = jnp.einsum(
        "qhk,khd->qhd",
        weights.astype(jnp.bfloat16),
        value_heads,
        preferred_element_type=jnp.float32,
    )
    if carry_state is not None:
        max_old, denom_old, numerator_old = carry_state
        rescale = jnp.exp(max_old - max_new)
        denom_new = denom_old * rescale + denom_new
        numerator = numerator_old * rescale[:, :, None] + numerator
    return (max_new, denom_new, numerator)


def shards(query_rows, key_rows, value_rows, utt_lengths, out_weight):
    frames = query_rows.shape[1]
    cycle_size = lax.axis_size("ctx")
    cycle_place = lax.axis_index("ctx")
    utt_ends = jnp.cumsum(utt_lengths[0])
    query_heads = query_rows[0].reshape(frames, HQ, HD)
    query_seg = segment_ids(utt_ends, cycle_place * frames, frames)

    def absorb(carry_state, kv_block, source, heads=slice(None)):
        key_seg = segment_ids(utt_ends, source * frames, frames)
        if not isinstance(kv_block, tuple):
            kv_block = (kv_block[0], kv_block[1])
        return attend(carry_state, query_heads[:, heads], query_seg, kv_block, key_seg)

    gathered_weight = lax.all_gather(out_weight, "dp", axis=0, tiled=True)
    kv_block = jnp.concatenate([key_rows, value_rows], axis=0)
    plane_size = cycle_size // 2
    plane = cycle_place // plane_size
    spot = cycle_place % plane_size

    def in_plane(block, step):
        route = [
            (i, (i // plane_size) * plane_size + (i % plane_size + step) % plane_size)
            for i in range(cycle_size)
        ]
        return lax.ppermute(block, "ctx", route)

    def around(block, source_plane):
        ahead = in_plane(block, 1)
        behind = in_plane(block, -1)
        far = (in_plane(ahead[0], 1), in_plane(behind[1], -1))
        base = source_plane * plane_size
        return [
            (ahead, base + (spot - 1) % plane_size),
            (behind, base + (spot + 1) % plane_size),
            (far, base + (spot + 2) % plane_size),
        ]

    partner = lax.ppermute(
        kv_block, "ctx", [(i, (i + plane_size) % cycle_size) for i in range(cycle_size)]
    )
    arrivals = [(kv_block, cycle_place)] + around(kv_block, plane)
    arrivals += [(partner, (cycle_place + plane_size) % cycle_size)]
    partner_ahead = in_plane(partner, 1)
    partner_behind = in_plane(partner, -1)
    arrivals += [
        (partner_ahead, (1 - plane) * plane_size + (spot - 1) % plane_size),
        (partner_behind, (1 - plane) * plane_size + (spot + 1) % plane_size),
    ]
    carry_state = None
    for block, source in arrivals:
        carry_state = lax.optimization_barrier(absorb(carry_state, block, source))
    far_source = (1 - plane) * plane_size + (spot + 2) % plane_size
    groups = 2
    width = HQ // groups
    pieces = []
    for group in range(groups):
        cols = slice(group * width * HD, (group + 1) * width * HD)
        pieces.append(
            (
                in_plane(partner_ahead[0][:, cols], 1),
                in_plane(partner_behind[1][:, cols], -1),
            )
        )
    summed = None
    for group in range(groups):
        heads = slice(group * width, (group + 1) * width)
        cols = slice(group * width * HD, (group + 1) * width * HD)
        if summed is not None:
            summed, pieces[group] = lax.optimization_barrier((summed, pieces[group]))
        far = pieces[group]
        group_state = tuple(part[:, heads] for part in carry_state)
        max_final, denom_final, numerator = absorb(group_state, far, far_source, heads)
        attn_rows = (numerator / denom_final[:, :, None]).reshape(frames, width * HD)
        partial = jnp.dot(
            attn_rows.astype(jnp.bfloat16),
            gathered_weight[cols],
            preferred_element_type=jnp.float32,
        )
        summed = partial if summed is None else summed + partial
    return summed.astype(jnp.bfloat16)[None]


def solution(mesh):
    return jax.shard_map(
        shards,
        mesh=mesh,
        in_specs=(
            P("dp", "ctx", None),
            P("dp", "ctx", None),
            P("dp", "ctx", None),
            P("dp", None),
            P("dp", None),
        ),
        out_specs=P("dp", "ctx", None),
        check_vma=False,
    )
```

```python
import jax
import jax.numpy as jnp
from jax import lax
from jax.sharding import PartitionSpec as P

HQ = 16
HD = 128


big_negative = -1e30


def segment_ids(utt_ends, first_frame, frames):
    positions = first_frame + jnp.arange(frames, dtype=jnp.int32)
    return jnp.sum((positions[:, None] >= utt_ends[None, :]).astype(jnp.int32), axis=1)


def attend(carry_state, query_heads, query_seg, kv_pair, key_seg):
    keys, values = kv_pair
    frames = keys.shape[0]
    key_heads = keys.reshape(frames, -1, HD)
    value_heads = values.reshape(frames, -1, HD)
    allowed = (query_seg[:, None] == key_seg[None, :])[:, None, :]
    scores = jnp.einsum(
        "qhd,khd->qhk", query_heads, key_heads, preferred_element_type=jnp.float32
    ) * HD ** (-0.5)
    masked = jnp.where(allowed, scores, big_negative)
    block_max = jnp.max(masked, axis=2)
    max_new = block_max if carry_state is None else jnp.maximum(carry_state[0], block_max)
    weights = jnp.exp(masked - max_new[:, :, None])
    denom_new = jnp.sum(weights, axis=2)
    numerator = jnp.einsum(
        "qhk,khd->qhd",
        weights.astype(jnp.bfloat16),
        value_heads,
        preferred_element_type=jnp.float32,
    )
    if carry_state is not None:
        max_old, denom_old, numerator_old = carry_state
        rescale = jnp.exp(max_old - max_new)
        denom_new = denom_old * rescale + denom_new
        numerator = numerator_old * rescale[:, :, None] + numerator
    return (max_new, denom_new, numerator)


def shards(query_rows, key_rows, value_rows, utt_lengths, out_weight):
    frames = query_rows.shape[1]
    cycle_size = lax.axis_size("ctx")
    cycle_place = lax.axis_index("ctx")
    utt_ends = jnp.cumsum(utt_lengths[0])
    query_heads = query_rows[0].reshape(frames, HQ, HD)
    query_seg = segment_ids(utt_ends, cycle_place * frames, frames)

    def absorb(carry_state, kv_block, source, heads=slice(None)):
        key_seg = segment_ids(utt_ends, source * frames, frames)
        if not isinstance(kv_block, tuple):
            kv_block = (kv_block[0], kv_block[1])
        return attend(carry_state, query_heads[:, heads], query_seg, kv_block, key_seg)

    gathered_weight = lax.all_gather(out_weight, "dp", axis=0, tiled=True)
    kv_block = jnp.concatenate([key_rows, value_rows], axis=0)
    plane_size = cycle_size // 2
    plane = cycle_place // plane_size
    spot = cycle_place % plane_size

    def in_plane(block, step):
        route = [
            (i, (i // plane_size) * plane_size + (i % plane_size + step) % plane_size)
            for i in range(cycle_size)
        ]
        return lax.ppermute(block, "ctx", route)

    def around(block, source_plane):
        ahead = in_plane(block, 1)
        behind = in_plane(block, -1)
        far = (in_plane(ahead[0], 1), in_plane(behind[1], -1))
        base = source_plane * plane_size
        return [
            (ahead, base + (spot - 1) % plane_size),
            (behind, base + (spot + 1) % plane_size),
            (far, base + (spot + 2) % plane_size),
        ]

    partner_route = [(i, (i + plane_size) % cycle_size) for i in range(cycle_size)]
    partner_keys = lax.ppermute(kv_block[0], "ctx", partner_route)
    own_values, partner_keys = lax.optimization_barrier((kv_block[1], partner_keys))
    partner_values = lax.ppermute(own_values, "ctx", partner_route)
    keys_ahead = in_plane(partner_keys, 1)
    keys_behind = in_plane(partner_keys, -1)
    values_ahead = in_plane(partner_values, 1)
    values_behind = in_plane(partner_values, -1)
    arrivals = [(kv_block, cycle_place)] + around(kv_block, plane)
    arrivals += [((partner_keys, partner_values), (cycle_place + plane_size) % cycle_size)]
    arrivals += [
        ((keys_ahead, values_ahead), (1 - plane) * plane_size + (spot - 1) % plane_size),
        ((keys_behind, values_behind), (1 - plane) * plane_size + (spot + 1) % plane_size),
    ]
    carry_state = None
    for block, source in arrivals:
        carry_state = lax.optimization_barrier(absorb(carry_state, block, source))
    far_source = (1 - plane) * plane_size + (spot + 2) % plane_size
    groups = 2
    width = HQ // groups
    pieces = []
    for group in range(groups):
        cols = slice(group * width * HD, (group + 1) * width * HD)
        step = 1 if group == 0 else -1
        keys_near = keys_ahead if group == 0 else keys_behind
        values_near = values_ahead if group == 0 else values_behind
        pieces.append(
            (in_plane(keys_near[:, cols], step), in_plane(values_near[:, cols], step))
        )
    summed = None
    for group in range(groups):
        heads = slice(group * width, (group + 1) * width)
        cols = slice(group * width * HD, (group + 1) * width * HD)
        if summed is not None:
            summed, pieces[group] = lax.optimization_barrier((summed, pieces[group]))
        far = pieces[group]
        group_state = tuple(part[:, heads] for part in carry_state)
        max_final, denom_final, numerator = absorb(group_state, far, far_source, heads)
        attn_rows = (numerator / denom_final[:, :, None]).reshape(frames, width * HD)
        partial = jnp.dot(
            attn_rows.astype(jnp.bfloat16),
            gathered_weight[cols],
            preferred_element_type=jnp.float32,
        )
        summed = partial if summed is None else summed + partial
    return summed.astype(jnp.bfloat16)[None]


def solution(mesh):
    return jax.shard_map(
        shards,
        mesh=mesh,
        in_specs=(
            P("dp", "ctx", None),
            P("dp", "ctx", None),
            P("dp", "ctx", None),
            P("dp", None),
            P("dp", None),
        ),
        out_specs=P("dp", "ctx", None),
        check_vma=False,
    )
```

```python
import jax
import jax.numpy as jnp
from jax import lax
from jax.sharding import PartitionSpec as P

HQ = 16
HD = 128


big_negative = -1e30


def segment_ids(utt_ends, first_frame, frames):
    positions = first_frame + jnp.arange(frames, dtype=jnp.int32)
    return jnp.sum((positions[:, None] >= utt_ends[None, :]).astype(jnp.int32), axis=1)


def attend(carry_state, query_heads, query_seg, kv_block, key_seg):
    frames = kv_block.shape[1]
    key_heads = kv_block[0].reshape(frames, -1, HD)
    value_heads = kv_block[1].reshape(frames, -1, HD)
    allowed = (query_seg[:, None] == key_seg[None, :])[:, None, :]
    scores = jnp.einsum(
        "qhd,khd->qhk", query_heads, key_heads, preferred_element_type=jnp.float32
    ) * HD ** (-0.5)
    masked = jnp.where(allowed, scores, big_negative)
    block_max = jnp.max(masked, axis=2)
    max_new = block_max if carry_state is None else jnp.maximum(carry_state[0], block_max)
    weights = jnp.exp(masked - max_new[:, :, None])
    denom_new = jnp.sum(weights, axis=2)
    numerator = jnp.einsum(
        "qhk,khd->qhd",
        weights.astype(jnp.bfloat16),
        value_heads,
        preferred_element_type=jnp.float32,
    )
    if carry_state is not None:
        max_old, denom_old, numerator_old = carry_state
        rescale = jnp.exp(max_old - max_new)
        denom_new = denom_old * rescale + denom_new
        numerator = numerator_old * rescale[:, :, None] + numerator
    return (max_new, denom_new, numerator)


def shards(query_rows, key_rows, value_rows, utt_lengths, out_weight):
    frames = query_rows.shape[1]
    cycle_size = lax.axis_size("ctx")
    cycle_place = lax.axis_index("ctx")
    utt_ends = jnp.cumsum(utt_lengths[0])
    query_heads = query_rows[0].reshape(frames, HQ, HD)
    query_seg = segment_ids(utt_ends, cycle_place * frames, frames)

    def absorb(carry_state, kv_block, source, heads=slice(None)):
        key_seg = segment_ids(utt_ends, source * frames, frames)
        return attend(carry_state, query_heads[:, heads], query_seg, kv_block, key_seg)

    gathered_weight = lax.all_gather(out_weight, "dp", axis=0, tiled=True)
    kv_block = jnp.concatenate([key_rows, value_rows], axis=0)
    plane_size = cycle_size // 2
    plane = cycle_place // plane_size
    spot = cycle_place % plane_size
    half = frames // 2

    def in_plane(block, step):
        route = [
            (i, (i // plane_size) * plane_size + (i % plane_size + step) % plane_size)
            for i in range(cycle_size)
        ]
        return lax.ppermute(block, "ctx", route)

    def around(block, source_plane):
        ahead = in_plane(block, 1)
        behind = in_plane(block, -1)
        ahead_two = in_plane(ahead[:, :half], 1)
        behind_two = in_plane(behind[:, half:], -1)
        far = jnp.concatenate([ahead_two, behind_two], axis=1)
        base = source_plane * plane_size
        return [
            (ahead, base + (spot - 1) % plane_size),
            (behind, base + (spot + 1) % plane_size),
            (far, base + (spot + 2) % plane_size),
        ]

    partner = lax.ppermute(
        kv_block, "ctx", [(i, (i + plane_size) % cycle_size) for i in range(cycle_size)]
    )
    arrivals = [(kv_block, cycle_place)] + around(kv_block, plane)
    arrivals += [(partner, (cycle_place + plane_size) % cycle_size)]
    partner_ahead = in_plane(partner, 1)
    partner_behind = in_plane(partner, -1)
    arrivals += [
        (partner_ahead, (1 - plane) * plane_size + (spot - 1) % plane_size),
        (partner_behind, (1 - plane) * plane_size + (spot + 1) % plane_size),
    ]
    carry_state = None
    for block, source in arrivals:
        carry_state = lax.optimization_barrier(absorb(carry_state, block, source))
    far_source = (1 - plane) * plane_size + (spot + 2) % plane_size
    groups = 2
    width = HQ // groups
    pieces = []
    for group in range(groups):
        cols = slice(group * width * HD, (group + 1) * width * HD)
        pieces.append(
            (
                in_plane(partner_ahead[:, :half, cols], 1),
                in_plane(partner_behind[:, half:, cols], -1),
            )
        )
    summed = None
    for group in range(groups):
        heads = slice(group * width, (group + 1) * width)
        cols = slice(group * width * HD, (group + 1) * width * HD)
        if summed is not None:
            summed, pieces[group] = lax.optimization_barrier((summed, pieces[group]))
        far = jnp.concatenate(pieces[group], axis=1)
        group_state = tuple(part[:, heads] for part in carry_state)
        max_final, denom_final, numerator = absorb(group_state, far, far_source, heads)
        attn_heads = (numerator / denom_final[:, :, None]).astype(jnp.bfloat16)
        partial = jnp.einsum(
            "qhd,hdn->qn",
            attn_heads,
            gathered_weight[cols].reshape(width, HD, -1),
            preferred_element_type=jnp.float32,
        )
        summed = partial if summed is None else summed + partial
    return summed.astype(jnp.bfloat16)[None]


def solution(mesh):
    return jax.shard_map(
        shards,
        mesh=mesh,
        in_specs=(
            P("dp", "ctx", None),
            P("dp", "ctx", None),
            P("dp", "ctx", None),
            P("dp", None),
            P("dp", None),
        ),
        out_specs=P("dp", "ctx", None),
        check_vma=False,
    )
```

```python
import jax
import jax.numpy as jnp
from jax import lax
from jax.sharding import PartitionSpec as P

HQ = 16
HD = 128


big_negative = -1e30


def segment_ids(utt_ends, first_frame, frames):
    positions = first_frame + jnp.arange(frames, dtype=jnp.int32)
    return jnp.sum((positions[:, None] >= utt_ends[None, :]).astype(jnp.int32), axis=1)


def attend(carry_state, query_heads, query_seg, kv_block, key_seg):
    frames = kv_block.shape[1]
    key_heads = kv_block[0].reshape(frames, -1, HD)
    value_heads = kv_block[1].reshape(frames, -1, HD)
    allowed = (query_seg[:, None] == key_seg[None, :])[:, None, :]
    scores = jnp.einsum(
        "qhd,khd->qhk", query_heads, key_heads, preferred_element_type=jnp.float32
    ) * HD ** (-0.5)
    masked = jnp.where(allowed, scores, big_negative)
    block_max = jnp.max(masked, axis=2)
    max_new = block_max if carry_state is None else jnp.maximum(carry_state[0], block_max)
    weights = jnp.exp(masked - max_new[:, :, None])
    denom_new = jnp.sum(weights, axis=2)
    numerator = jnp.einsum(
        "qhk,khd->qhd",
        weights.astype(jnp.bfloat16),
        value_heads,
        preferred_element_type=jnp.float32,
    )
    if carry_state is not None:
        max_old, denom_old, numerator_old = carry_state
        rescale = jnp.exp(max_old - max_new)
        denom_new = denom_old * rescale + denom_new
        numerator = numerator_old * rescale[:, :, None] + numerator
    return (max_new, denom_new, numerator)


def shards(query_rows, key_rows, value_rows, utt_lengths, out_weight):
    frames = query_rows.shape[1]
    cycle_size = lax.axis_size("ctx")
    cycle_place = lax.axis_index("ctx")
    utt_ends = jnp.cumsum(utt_lengths[0])
    query_heads = query_rows[0].reshape(frames, HQ, HD)
    query_seg = segment_ids(utt_ends, cycle_place * frames, frames)

    def absorb(carry_state, kv_block, source, heads=slice(None)):
        key_seg = segment_ids(utt_ends, source * frames, frames)
        return attend(carry_state, query_heads[:, heads], query_seg, kv_block, key_seg)

    gathered_weight = lax.all_gather(out_weight, "dp", axis=0, tiled=True)
    kv_block = jnp.concatenate([key_rows, value_rows], axis=0)
    plane_size = cycle_size // 2
    plane = cycle_place // plane_size
    spot = cycle_place % plane_size
    half = frames // 2

    def in_plane(block, step):
        route = [
            (i, (i // plane_size) * plane_size + (i % plane_size + step) % plane_size)
            for i in range(cycle_size)
        ]
        return lax.ppermute(block, "ctx", route)

    def around(block, source_plane):
        ahead = in_plane(block, 1)
        behind = in_plane(block, -1)
        ahead_two = in_plane(ahead[:, :half], 1)
        behind_two = in_plane(behind[:, half:], -1)
        far = jnp.concatenate([ahead_two, behind_two], axis=1)
        base = source_plane * plane_size
        return [
            (ahead, base + (spot - 1) % plane_size),
            (behind, base + (spot + 1) % plane_size),
            (far, base + (spot + 2) % plane_size),
        ]

    partner = lax.ppermute(
        kv_block, "ctx", [(i, (i + plane_size) % cycle_size) for i in range(cycle_size)]
    )
    arrivals = [(kv_block, cycle_place)] + around(kv_block, plane)
    arrivals += [(partner, (cycle_place + plane_size) % cycle_size)]
    partner_ahead = in_plane(partner, 1)
    partner_behind = in_plane(partner, -1)
    arrivals += [
        (partner_ahead, (1 - plane) * plane_size + (spot - 1) % plane_size),
        (partner_behind, (1 - plane) * plane_size + (spot + 1) % plane_size),
    ]
    carry_state = None
    for block, source in arrivals:
        carry_state = lax.optimization_barrier(absorb(carry_state, block, source))
    far_source = (1 - plane) * plane_size + (spot + 2) % plane_size
    bounds = (0, HQ * 3 // 4, HQ)
    groups = len(bounds) - 1
    pieces = []
    for group in range(groups):
        cols = slice(bounds[group] * HD, bounds[group + 1] * HD)
        pieces.append(
            (
                in_plane(partner_ahead[:, :half, cols], 1),
                in_plane(partner_behind[:, half:, cols], -1),
            )
        )
    summed = None
    for group in range(groups):
        heads = slice(bounds[group], bounds[group + 1])
        cols = slice(bounds[group] * HD, bounds[group + 1] * HD)
        if summed is not None:
            summed, pieces[group] = lax.optimization_barrier((summed, pieces[group]))
        far = jnp.concatenate(pieces[group], axis=1)
        group_state = tuple(part[:, heads] for part in carry_state)
        max_final, denom_final, numerator = absorb(group_state, far, far_source, heads)
        attn_rows = (numerator / denom_final[:, :, None]).reshape(frames, -1)
        partial = jnp.dot(
            attn_rows.astype(jnp.bfloat16),
            gathered_weight[cols],
            preferred_element_type=jnp.float32,
        )
        summed = partial if summed is None else summed + partial
    return summed.astype(jnp.bfloat16)[None]


def solution(mesh):
    return jax.shard_map(
        shards,
        mesh=mesh,
        in_specs=(
            P("dp", "ctx", None),
            P("dp", "ctx", None),
            P("dp", "ctx", None),
            P("dp", None),
            P("dp", None),
        ),
        out_specs=P("dp", "ctx", None),
        check_vma=False,
    )
```
